512 devices in a mesh: dp: 64 (over z, x_hi, core), fsdp: 8 (over x_lo, y).
Axes of the slice: x: 4 (x_hi: 2, x_lo: 2; x = x_hi * 2 + x_lo), y: 4, z: 16, core: 2. Of those that a mesh axis runs over, the one named last changes fastest.
Arguments:
- states: bfloat16 [128, 512, 5120], P('dp', None, 'fsdp'), may hold values from -240 to 240
- valid_counts: int32 [128], P('dp'), may hold values from 32 to 512
- section_ids: int32 [128], replicated, may hold values from 0 to 63, never falling along the last dimension, each value on 1 to 6 neighbouring positions
- norm_gain: bfloat16 [5120], P('fsdp'), may hold values from 0.099609375 to 1.8984375
- head_weight: bfloat16 [5120, 2048], P('fsdp'), may hold values from -0.078125 to 0.078125
Outputs:
- embeddings: float32 [64, 3840], P('dp')
The draws below stay inside these ranges and needn't reach their ends.
Inputs may be any that keep to these rules, and one draw needn't show every extreme that they name: `section_ids`: section numbers never fall along the spans; every one of the 64 sections has 1 to 6 spans.
All inputs are finite; a program needn't handle non-finite values.
Results may differ from the reference program's by a relative error of at most 0.0003.
Values sent between devices are 32-bit elements; how exact they have to be, the bound alone decides.
No kernel may reach another device: no remote copies, remote signals or barrier semaphores. Data moves between devices by JAX's collectives and lax.ppermute only.
A program may use at most 64 MiB of HBM per device.

```python
import math
import jax
import jax.numpy as jnp
import numpy as np
from jax import lax

D = 5120
M = 2048
SPAN_LEN = 512
SPANS = 128
SECTIONS = 64


def draw_states(key, part):
    keys = jax.random.split(key, 3)
    shape = (SPANS, SPAN_LEN, D)
    ramp = 3.0 ** (jnp.arange(D, dtype=jnp.float32) / D)
    column = 10.0 ** jax.random.uniform(keys[1], (D,), jnp.float32, -0.5, 0.5)
    rowwise = 10.0 ** jax.random.uniform(keys[2], (SPANS, SPAN_LEN, 1), jnp.float32, -0.5, 0.5)
    base = jax.random.normal(keys[0], shape, jnp.float32)
    base = jnp.clip(base, -6.0, 6.0)
    return (base * rowwise * column * ramp).astype(jnp.bfloat16)


def plant(values, stream_key, smallest, high):
    dims = values.shape
    spot = [jax.random.randint(jax.random.fold_in(stream_key, axis), (), 0, dims[axis]) for axis in range(len(dims))]
    values = values.at[tuple(spot)].set(smallest)
    longest = dims.index(max(dims))
    spot[longest] = (spot[longest] + 1) % dims[longest]
    return values.at[tuple(spot)].set(high)


def levels(stream_key, shape, cuts, low, largest):
    loudness, own = 1.0, jax.random.fold_in(stream_key, 6)
    for axis_at, blocks in cuts:
        heights = jnp.exp(jax.random.uniform(jax.random.fold_in(own, axis_at), (blocks,), jnp.float32, low / len(cuts), largest / len(cuts)))
        loudness = loudness * jnp.repeat(heights, shape[axis_at] // blocks).reshape([-1 if axis == axis_at else 1 for axis in range(len(shape))])
    return loudness


def length_profile(number_of, total, limit, skew):
    portions = [(1 << 20) // math.isqrt(standing ** skew) + 1 for standing in range(2, number_of + 1)]
    surplus, counts = total - limit - (number_of - 1), [1] * (number_of - 1)
    while surplus > 0:
        candidates = [i for i in range(number_of - 1) if counts[i] < limit]
        mass, remaining = sum([portions[i] for i in candidates]), surplus
        for i in candidates:
            more = min(limit - counts[i], max(1, remaining * portions[i] // mass), surplus)
            counts[i] = counts[i] + more
            surplus = surplus - more
    return np.array([limit] + counts)


def uneven_parts(own_key, count, total, bound, skew):
    if count == 2:
        one = jax.random.randint(own_key, (), max(1, total - bound), min(bound, total - 1) + 1)
        return jnp.stack([one, total - one])
    lengths = jnp.asarray(length_profile(count, total, bound, skew), jnp.int32)
    twos = (count - 1) // 2
    source_of, taker = lengths[1:1 + 2 * twos:2], lengths[2:2 + 2 * twos:2]
    room = jnp.minimum(source_of - 1, bound - taker)
    passed = jax.random.randint(jax.random.fold_in(own_key, 1), (twos,), 0, 1 << 20) % (room + 1)
    lengths = lengths.at[1:1 + 2 * twos:2].set(source_of - passed).at[2:2 + 2 * twos:2].set(taker + passed)
    return lengths[jax.random.permutation(jax.random.fold_in(own_key, 2), count)]


def noise(rng, dims, spread, bound, cuts=(), kind=jnp.bfloat16):
    entries = jax.random.normal(rng, dims, jnp.float32) * spread
    if len(cuts) > 0:
        entries = levels(rng, dims, cuts, -0.22, 0.18) * entries
    return jnp.clip(entries, min=-bound, max=bound).astype(kind)


def setup_inputs(seed: int = 0) -> dict:
    seeds = jax.random.split(jax.random.key(seed), 6)
    return {
        "states": draw_states(jax.random.fold_in(seeds[5], 71), 0),
        "valid_counts": plant(jax.random.randint(seeds[1], (SPANS,), max(1, SPAN_LEN // 16), SPAN_LEN + 1), jax.random.fold_in(seeds[1], 1), max(1, SPAN_LEN // 16), SPAN_LEN).astype(jnp.int32),
        "section_ids": jnp.searchsorted(jnp.cumsum(uneven_parts(seeds[2], SECTIONS, SPANS, 6, 1)), jnp.arange(SPANS), side="right").astype(jnp.int32),
        "norm_gain": jnp.clip(1.0 + 0.18 * jax.random.normal(seeds[3], (D,), jnp.float32), 0.099609375, 1.8984375).astype(jnp.bfloat16),
        "head_weight": noise(seeds[4], (D, M), D ** -0.5, 0.078125, ((0, 8),)),
    }


epsilon = 1e-06

def pool_span(item):
    block, count = item
    values = block.astype(jnp.float32)
    squares = lax.optimization_barrier(jnp.sum(values * values, axis=-1))
    scale = lax.rsqrt(squares / D + epsilon)
    slots = jnp.arange(SPAN_LEN, dtype=jnp.int32)
    used = (slots < count).astype(jnp.float32)
    weights = scale * used
    return lax.optimization_barrier(jnp.sum(values * weights[:, None], axis=0)) / count.astype(jnp.float32)

def reference(states, valid_counts, section_ids, norm_gain, head_weight):
    pooled = lax.map(pool_span, (states, valid_counts))
    pooled = pooled * norm_gain.astype(jnp.float32)[None, :]
    labels = jnp.arange(SECTIONS, dtype=jnp.int32)
    member = (section_ids[None, :] == labels[:, None]).astype(jnp.float32)
    section_sums = jnp.dot(member, pooled, precision=lax.Precision.HIGHEST)
    projected = jnp.dot(section_sums, head_weight.astype(jnp.float32), precision=lax.Precision.HIGHEST)
    pieces = []
    for level in (M // 8, M // 4, M // 2, M):
        front = projected[:, :level]
        pieces.append(front * lax.rsqrt(lax.optimization_barrier(jnp.mean(front * front, axis=1, keepdims=True)) + epsilon))
    return jnp.concatenate(pieces, axis=1)
```

```python
import jax
import jax.numpy as jnp
from jax import lax
from jax.sharding import PartitionSpec as P

D = 5120


epsilon = 1e-06


def nested(projected):
    width = projected.shape[1]
    pieces = []
    for level in (width // 8, width // 4, width // 2, width):
        front = projected[:, :level]
        pieces.append(front * lax.rsqrt(jnp.mean(front * front, axis=1, keepdims=True) + epsilon))
    return jnp.concatenate(pieces, axis=1)


def local(states, valid_counts, section_ids, norm_gain, head_weight):
    values = states.astype(jnp.float32)
    partial_squares = jnp.sum(values * values, axis=-1)
    squares = lax.psum(partial_squares, "fsdp")
    scale = lax.rsqrt(squares / D + epsilon)
    slots = jnp.arange(states.shape[1], dtype=jnp.int32)
    used = (slots[None, :] < valid_counts[:, None]).astype(jnp.float32)
    weights = scale * used
    sums = jnp.einsum("cl,cld->cd", weights, values, precision=lax.Precision.HIGHEST)
    pooled = (
        sums / valid_counts.astype(jnp.float32)[:, None] * norm_gain.astype(jnp.float32)[None, :]
    )
    groups = lax.axis_size("dp")
    local_spans = pooled.shape[0]
    sec_local = local_spans // 2
    total_sections = sec_local * groups
    me = lax.axis_index("dp")
    my_ids = lax.dynamic_slice_in_dim(section_ids, me * local_spans, local_spans, 0)
    labels = jnp.arange(total_sections, dtype=jnp.int32)
    contrib = jnp.zeros((total_sections, pooled.shape[1]), jnp.float32)
    for c in range(local_spans):
        contrib = contrib + jnp.where((labels == my_ids[c])[:, None], pooled[c][None, :], 0.0)
    received = lax.all_to_all(contrib, "dp", 0, 0, tiled=True)
    section_sums = jnp.sum(received.reshape(groups, sec_local, -1), axis=0)
    terms = jnp.dot(section_sums, head_weight.astype(jnp.float32), precision=lax.Precision.HIGHEST)
    projected = lax.psum(terms, "fsdp")
    return nested(projected)


def solution(mesh):
    in_specs = (P("dp", None, "fsdp"), P("dp"), P(), P("fsdp"), P("fsdp", None))
    out_specs = P("dp", None)
    return jax.shard_map(local, mesh=mesh, in_specs=in_specs, out_specs=out_specs, check_vma=False)
```

```python
import jax
import jax.numpy as jnp
from jax import lax
from jax.experimental import pallas as pl
from jax.sharding import Mesh, PartitionSpec as P

D = 5120


epsilon = 1e-06


def nested_kernel(x_ref, o_ref):
    x = x_ref[...]
    width = x.shape[1]
    squared = x * x
    offset = 0
    for level in (width // 8, width // 4, width // 2, width):
        mean = jnp.sum(squared[:, :level], axis=1, keepdims=True) / level
        o_ref[:, offset:offset + level] = x[:, :level] * lax.rsqrt(mean + epsilon)
        offset += level


def nested(projected):
    rows, width = projected.shape
    out = jax.ShapeDtypeStruct((rows, width // 8 + width // 4 + width // 2 + width), jnp.float32)
    return pl.pallas_call(nested_kernel, out_shape=out)(projected)


def fsdp_sum(x):
    return lax.psum(lax.psum(x, "y"), "xl")


def local(states, valid_counts, section_ids, norm_gain, head_weight):
    values = states.astype(jnp.float32)
    partial_squares = jnp.sum(values * values, axis=-1)
    squares = fsdp_sum(partial_squares)
    scale = lax.rsqrt(squares / D + epsilon)
    slots = jnp.arange(states.shape[1], dtype=jnp.int32)
    used = (slots[None, :] < valid_counts[:, None]).astype(jnp.float32)
    weights = scale * used
    sums = jnp.einsum("cl,cld->cd", weights, values, precision=lax.Precision.HIGHEST)
    pooled = (
        sums / valid_counts.astype(jnp.float32)[:, None] * norm_gain.astype(jnp.float32)[None, :]
    )
    groups = lax.axis_size("dp")
    local_spans = pooled.shape[0]
    sec_local = local_spans // 2
    total_sections = sec_local * groups
    me = lax.axis_index("dp")
    my_ids = lax.dynamic_slice_in_dim(section_ids, me * local_spans, local_spans, 0)
    labels = jnp.arange(total_sections, dtype=jnp.int32)
    contrib = jnp.zeros((total_sections, pooled.shape[1]), jnp.float32)
    for c in range(local_spans):
        contrib = contrib + jnp.where((labels == my_ids[c])[:, None], pooled[c][None, :], 0.0)
    received = lax.all_to_all(contrib, "dp", 0, 0, tiled=True)
    section_sums = jnp.sum(received.reshape(groups, sec_local, -1), axis=0)
    terms = jnp.dot(section_sums, head_weight.astype(jnp.float32), precision=lax.Precision.HIGHEST)
    projected = fsdp_sum(terms)
    return nested(projected)


def solution(mesh):
    dp, fsdp = mesh.shape["dp"], mesh.shape["fsdp"]
    fine = Mesh(mesh.devices.reshape(dp, 2, fsdp // 2), ("dp", "xl", "y"))
    features = ("xl", "y")
    in_specs = (P("dp", None, features), P("dp"), P(), P(features), P(features, None))
    out_specs = P("dp", None)
    return jax.shard_map(local, mesh=fine, in_specs=in_specs, out_specs=out_specs, check_vma=False)
```

```python
import jax
import jax.numpy as jnp
from jax import lax
from jax.experimental import pallas as pl
from jax.experimental.pallas import tpu as pltpu
from jax.sharding import Mesh, PartitionSpec as P

D = 5120


epsilon = 1e-06


def nested_kernel(x_ref, o_ref):
    x = x_ref[...]
    width = x.shape[1]
    squared = x * x
    offset = 0
    for level in (width // 8, width // 4, width // 2, width):
        mean = jnp.sum(squared[:, :level], axis=1, keepdims=True) / level
        o_ref[:, offset:offset + level] = x[:, :level] * lax.rsqrt(mean + epsilon)
        offset += level


def nested(projected):
    rows, width = projected.shape
    out = jax.ShapeDtypeStruct((rows, width // 8 + width // 4 + width // 2 + width), jnp.float32)
    return pl.pallas_call(nested_kernel, out_shape=out)(projected)


def fsdp_sum(x):
    return lax.psum(lax.psum(x, "y"), "xl")


def pool_kernel(counts_ref, ids_ref, states_ref, squares_ref, gain_ref, out_ref):
    spans, slots_n, _ = states_ref.shape
    me = lax.axis_index("dp")
    out_ref[...] = jnp.zeros(out_ref.shape, jnp.float32)
    gain = gain_ref[...].astype(jnp.float32)
    for c in range(spans):
        count = counts_ref[c]
        scale = lax.rsqrt(squares_ref[pl.ds(c, 1), :] / D + epsilon)
        slots = lax.broadcasted_iota(jnp.int32, scale.shape, 1)
        weights = jnp.where(slots < count, scale, 0.0)
        column = jnp.transpose(jnp.broadcast_to(weights, (128, slots_n)))[:, :1]
        values = states_ref[c].astype(jnp.float32)
        sums = jnp.sum(values * column, axis=0, keepdims=True)
        pooled = sums / count.astype(jnp.float32) * gain
        section = ids_ref[me * spans + c]
        out_ref[pl.ds(section, 1)] += pooled[None]


def local(states, valid_counts, section_ids, norm_gain, head_weight):
    values = states.astype(jnp.float32)
    partial_squares = jnp.sum(values * values, axis=-1)
    squares = fsdp_sum(partial_squares)
    groups = lax.axis_size("dp")
    local_spans, _, features = states.shape
    sec_local = local_spans // 2
    total_sections = sec_local * groups
    smem = pl.BlockSpec(memory_space=pltpu.SMEM)
    vmem = pl.BlockSpec(memory_space=pltpu.VMEM)
    contrib = pl.pallas_call(
        pool_kernel,
        out_shape=jax.ShapeDtypeStruct((total_sections, 1, features), jnp.float32),
        in_specs=[smem, smem, vmem, vmem, vmem],
        out_specs=vmem,
    )(valid_counts, section_ids, states, squares, norm_gain.reshape(1, features))
    received = lax.all_to_all(contrib, "dp", 0, 0, tiled=True)
    section_sums = jnp.sum(received.reshape(groups, sec_local, features), axis=0)
    terms = jnp.dot(section_sums, head_weight.astype(jnp.float32), precision=lax.Precision.HIGHEST)
    projected = fsdp_sum(terms)
    return nested(projected)


def solution(mesh):
    dp, fsdp = mesh.shape["dp"], mesh.shape["fsdp"]
    fine = Mesh(mesh.devices.reshape(dp, 2, fsdp // 2), ("dp", "xl", "y"))
    features = ("xl", "y")
    in_specs = (P("dp", None, features), P("dp"), P(), P(features), P(features, None))
    out_specs = P("dp", None)
    return jax.shard_map(local, mesh=fine, in_specs=in_specs, out_specs=out_specs, check_vma=False)
```

```python
import functools

import jax
import jax.numpy as jnp
from jax import lax
from jax.experimental import pallas as pl
from jax.experimental.pallas import tpu as pltpu
from jax.sharding import Mesh, PartitionSpec as P

D = 5120


epsilon = 1e-06


def nested_kernel(x_ref, o_ref):
    x = x_ref[...]
    width = x.shape[1]
    squared = x * x
    offset = 0
    for level in (width // 8, width // 4, width // 2, width):
        mean = jnp.sum(squared[:, :level], axis=1, keepdims=True) / level
        o_ref[:, offset:offset + level] = x[:, :level] * lax.rsqrt(mean + epsilon)
        offset += level


def nested(projected):
    rows, width = projected.shape
    out = jax.ShapeDtypeStruct((rows, width // 8 + width // 4 + width // 2 + width), jnp.float32)
    return pl.pallas_call(nested_kernel, out_shape=out)(projected)


def fsdp_sum(x):
    return lax.psum(lax.psum(x, "y"), "xl")


def pool_kernel(dp_shape, counts_ref, ids_ref, states_ref, squares_ref, out_ref):
    spans, slots_n, _ = states_ref.shape
    z_n, xh_n, c_n = dp_shape
    sec_local = out_ref.shape[0] // (z_n * xh_n * c_n)
    me = (lax.axis_index("z") * xh_n + lax.axis_index("xh")) * c_n + lax.axis_index("c")
    out_ref[...] = jnp.zeros(out_ref.shape, jnp.float32)
    for c in range(spans):
        count = counts_ref[c]
        scale = lax.rsqrt(squares_ref[pl.ds(c, 1), :] / D + epsilon)
        slots = lax.broadcasted_iota(jnp.int32, scale.shape, 1)
        weights = jnp.where(slots < count, scale, 0.0)
        column = jnp.transpose(jnp.broadcast_to(weights, (128, slots_n)))[:, :1]
        values = states_ref[c].astype(jnp.float32)
        sums = jnp.sum(values * column, axis=0, keepdims=True)
        pooled = sums / count.astype(jnp.float32)
        section = ids_ref[me * spans + c]
        owner = section // sec_local
        place = ((owner % c_n) * xh_n + (owner // c_n) % xh_n) * z_n + owner // (c_n * xh_n)
        row = place * sec_local + section % sec_local
        out_ref[pl.ds(row, 1)] += pooled[None]


def make_local(dp_shape):
    groups = dp_shape[0] * dp_shape[1] * dp_shape[2]

    def local(states, valid_counts, section_ids, norm_gain, head_weight):
        values = states.astype(jnp.float32)
        partial_squares = jnp.sum(values * values, axis=-1)
        squares = fsdp_sum(partial_squares)
        local_spans, _, features = states.shape
        sec_local = local_spans // 2
        total_sections = sec_local * groups
        smem = pl.BlockSpec(memory_space=pltpu.SMEM)
        vmem = pl.BlockSpec(memory_space=pltpu.VMEM)
        contrib = pl.pallas_call(
            functools.partial(pool_kernel, dp_shape),
            out_shape=jax.ShapeDtypeStruct((total_sections, 1, features), jnp.float32),
            in_specs=[smem, smem, vmem, vmem],
            out_specs=vmem,
        )(valid_counts, section_ids, states, squares)
        received = lax.all_to_all(contrib, ("c", "xh", "z"), 0, 0, tiled=True)
        section_sums = jnp.sum(received.reshape(groups, sec_local, features), axis=0)
        section_sums = section_sums * norm_gain.astype(jnp.float32)[None, :]
        terms = jnp.dot(section_sums, head_weight.astype(jnp.float32), precision=lax.Precision.HIGHEST)
        projected = fsdp_sum(terms)
        return nested(projected)

    return local


def solution(mesh):
    dp, fsdp = mesh.shape["dp"], mesh.shape["fsdp"]
    dp_shape = (dp // 4, 2, 2)
    fine = Mesh(mesh.devices.reshape(*dp_shape, 2, fsdp // 2), ("z", "xh", "c", "xl", "y"))
    spans = ("z", "xh", "c")
    features = ("xl", "y")
    in_specs = (P(spans, None, features), P(spans), P(), P(features), P(features, None))
    out_specs = P(spans, None)
    return jax.shard_map(make_local(dp_shape), mesh=fine, in_specs=in_specs, out_specs=out_specs, check_vma=False)
```

```python
import functools

import jax
import jax.numpy as jnp
from jax import lax
from jax.experimental import pallas as pl
from jax.experimental.pallas import tpu as pltpu
from jax.sharding import Mesh, PartitionSpec as P

D = 5120


epsilon = 1e-06


def nested_kernel(x_ref, o_ref):
    x = x_ref[...]
    width = x.shape[1]
    squared = x * x
    offset = 0
    for level in (width // 8, width // 4, width // 2, width):
        mean = jnp.sum(squared[:, :level], axis=1, keepdims=True) / level
        o_ref[:, offset:offset + level] = x[:, :level] * lax.rsqrt(mean + epsilon)
        offset += level


def nested(projected):
    rows, width = projected.shape
    out = jax.ShapeDtypeStruct((rows, width // 8 + width // 4 + width // 2 + width), jnp.float32)
    return pl.pallas_call(nested_kernel, out_shape=out)(projected)


def fsdp_sum(x):
    return lax.psum(lax.psum(x, "y"), "xl")


def pool_kernel(dp_shape, counts_ref, ids_ref, states_ref, squares_ref, out_ref):
    spans, slots_n, _ = states_ref.shape
    z_n, xh_n, c_n = dp_shape
    sec_local = out_ref.shape[0] // (z_n * xh_n * c_n)
    me = (lax.axis_index("z") * xh_n + lax.axis_index("xh")) * c_n + lax.axis_index("c")
    out_ref[...] = jnp.zeros(out_ref.shape, jnp.float32)
    for c in range(spans):
        count = counts_ref[c]
        scale = lax.rsqrt(squares_ref[pl.ds(c, 1), :] / D + epsilon)
        slots = lax.broadcasted_iota(jnp.int32, scale.shape, 1)
        weights = jnp.where(slots < count, scale, 0.0)
        column = jnp.transpose(jnp.broadcast_to(weights, (128, slots_n)))[:, :1]
        values = states_ref[c].astype(jnp.float32)
        sums = jnp.sum(values * column, axis=0, keepdims=True)
        pooled = sums / count.astype(jnp.float32)
        section = ids_ref[me * spans + c]
        owner = section // sec_local
        place = ((owner % c_n) * xh_n + (owner // c_n) % xh_n) * z_n + owner // (c_n * xh_n)
        row = place * sec_local + section % sec_local
        out_ref[pl.ds(row, 1)] += pooled[None]


def squares_kernel(states_ref, out_ref):
    spans, slots_n, _ = states_ref.shape
    for c in range(spans):
        values = states_ref[c].astype(jnp.float32)
        column = jnp.sum(values * values, axis=1, keepdims=True)
        out_ref[pl.ds(c, 1), :] = jnp.transpose(jnp.broadcast_to(column, (slots_n, 128)))[:1, :]


def make_local(dp_shape):
    groups = dp_shape[0] * dp_shape[1] * dp_shape[2]

    def local(states, valid_counts, section_ids, norm_gain, head_weight):
        local_spans, slots_n, features = states.shape
        partial_squares = pl.pallas_call(
            squares_kernel, out_shape=jax.ShapeDtypeStruct((local_spans, slots_n), jnp.float32)
        )(states)
        squares = fsdp_sum(partial_squares)
        sec_local = local_spans // 2
        total_sections = sec_local * groups
        smem = pl.BlockSpec(memory_space=pltpu.SMEM)
        vmem = pl.BlockSpec(memory_space=pltpu.VMEM)
        contrib = pl.pallas_call(
            functools.partial(pool_kernel, dp_shape),
            out_shape=jax.ShapeDtypeStruct((total_sections, 1, features), jnp.float32),
            in_specs=[smem, smem, vmem, vmem],
            out_specs=vmem,
        )(valid_counts, section_ids, states, squares)
        received = lax.all_to_all(contrib, ("c", "xh", "z"), 0, 0, tiled=True)
        section_sums = jnp.sum(received.reshape(groups, sec_local, features), axis=0)
        section_sums = section_sums * norm_gain.astype(jnp.float32)[None, :]
        terms = jnp.dot(section_sums, head_weight.astype(jnp.float32), precision=lax.Precision.HIGHEST)
        projected = fsdp_sum(terms)
        return nested(projected)

    return local


def solution(mesh):
    dp, fsdp = mesh.shape["dp"], mesh.shape["fsdp"]
    dp_shape = (dp // 4, 2, 2)
    fine = Mesh(mesh.devices.reshape(*dp_shape, 2, fsdp // 2), ("z", "xh", "c", "xl", "y"))
    spans = ("z", "xh", "c")
    features = ("xl", "y")
    in_specs = (P(spans, None, features), P(spans), P(), P(features), P(features, None))
    out_specs = P(spans, None)
    return jax.shard_map(make_local(dp_shape), mesh=fine, in_specs=in_specs, out_specs=out_specs, check_vma=False)
```

```python
import functools

import jax
import jax.numpy as jnp
from jax import lax
from jax.experimental import pallas as pl
from jax.experimental.pallas import tpu as pltpu
from jax.sharding import Mesh, PartitionSpec as P

D = 5120


epsilon = 1e-06


def nested_kernel(x_ref, o_ref):
    x = x_ref[...]
    width = x.shape[1]
    squared = x * x
    offset = 0
    for level in (width // 8, width // 4, width // 2, width):
        mean = jnp.sum(squared[:, :level], axis=1, keepdims=True) / level
        o_ref[:, offset:offset + level] = x[:, :level] * lax.rsqrt(mean + epsilon)
        offset += level


def nested(projected):
    rows, width = projected.shape
    out = jax.ShapeDtypeStruct((rows, width // 8 + width // 4 + width // 2 + width), jnp.float32)
    return pl.pallas_call(nested_kernel, out_shape=out)(projected)


def fsdp_sum(x):
    return lax.psum(lax.psum(x, "y"), "xl")


def pool_kernel(dp_shape, counts_ref, ids_ref, states_ref, squares_ref, out_ref):
    spans, slots_n, _ = states_ref.shape
    z_n, xh_n, c_n = dp_shape
    sec_local = out_ref.shape[0] // (z_n * xh_n * c_n)
    me = (lax.axis_index("z") * xh_n + lax.axis_index("xh")) * c_n + lax.axis_index("c")
    out_ref[...] = jnp.zeros(out_ref.shape, jnp.float32)
    rows = lax.broadcasted_iota(jnp.int32, (8, slots_n), 0)
    for c in range(spans):
        count = counts_ref[c]
        scale = lax.rsqrt(squares_ref[pl.ds(c, 1), :] / D + epsilon)
        slots = lax.broadcasted_iota(jnp.int32, scale.shape, 1)
        weights = jnp.where(slots < count, scale, 0.0)
        high = weights.astype(jnp.bfloat16)
        rest = weights - high.astype(jnp.float32)
        middle = rest.astype(jnp.bfloat16)
        low = (rest - middle.astype(jnp.float32)).astype(jnp.bfloat16)
        zero = jnp.zeros_like(high)
        parts = jnp.where(rows == 0, high, jnp.where(rows == 1, middle, jnp.where(rows == 2, low, zero)))
        partial = jnp.dot(parts, states_ref[c], preferred_element_type=jnp.float32)
        sums = partial[0:1, :] + partial[1:2, :] + partial[2:3, :]
        pooled = sums / count.astype(jnp.float32)
        section = ids_ref[me * spans + c]
        owner = section // sec_local
        place = ((owner % c_n) * xh_n + (owner // c_n) % xh_n) * z_n + owner // (c_n * xh_n)
        row = place * sec_local + section % sec_local
        out_ref[pl.ds(row, 1)] += pooled[None]


def make_local(dp_shape):
    groups = dp_shape[0] * dp_shape[1] * dp_shape[2]

    def local(states, valid_counts, section_ids, norm_gain, head_weight):
        values = states.astype(jnp.float32)
        partial_squares = jnp.sum(values * values, axis=-1)
        squares = fsdp_sum(partial_squares)
        local_spans, _, features = states.shape
        sec_local = local_spans // 2
        total_sections = sec_local * groups
        smem = pl.BlockSpec(memory_space=pltpu.SMEM)
        vmem = pl.BlockSpec(memory_space=pltpu.VMEM)
        contrib = pl.pallas_call(
            functools.partial(pool_kernel, dp_shape),
            out_shape=jax.ShapeDtypeStruct((total_sections, 1, features), jnp.float32),
            in_specs=[smem, smem, vmem, vmem],
            out_specs=vmem,
        )(valid_counts, section_ids, states, squares)
        received = lax.all_to_all(contrib, ("c", "xh", "z"), 0, 0, tiled=True)
        section_sums = jnp.sum(received.reshape(groups, sec_local, features), axis=0)
        section_sums = section_sums * norm_gain.astype(jnp.float32)[None, :]
        terms = jnp.dot(section_sums, head_weight.astype(jnp.float32), precision=lax.Precision.HIGHEST)
        projected = fsdp_sum(terms)
        return nested(projected)

    return local


def solution(mesh):
    dp, fsdp = mesh.shape["dp"], mesh.shape["fsdp"]
    dp_shape = (dp // 4, 2, 2)
    fine = Mesh(mesh.devices.reshape(*dp_shape, 2, fsdp // 2), ("z", "xh", "c", "xl", "y"))
    spans = ("z", "xh", "c")
    features = ("xl", "y")
    in_specs = (P(spans, None, features), P(spans), P(), P(features), P(features, None))
    out_specs = P(spans, None)
    return jax.shard_map(make_local(dp_shape), mesh=fine, in_specs=in_specs, out_specs=out_specs, check_vma=False)
```

```python
import functools

import jax
import jax.numpy as jnp
from jax import lax
from jax.experimental import pallas as pl
from jax.experimental.pallas import tpu as pltpu
from jax.sharding import Mesh, PartitionSpec as P

D = 5120


epsilon = 1e-06


def nested_kernel(x_ref, o_ref):
    x = x_ref[...]
    width = x.shape[1]
    squared = x * x
    offset = 0
    for level in (width // 8, width // 4, width // 2, width):
        mean = jnp.sum(squared[:, :level], axis=1, keepdims=True) / level
        o_ref[:, offset:offset + level] = x[:, :level] * lax.rsqrt(mean + epsilon)
        offset += level


def nested(projected):
    rows, width = projected.shape
    out = jax.ShapeDtypeStruct((rows, width // 8 + width // 4 + width // 2 + width), jnp.float32)
    return pl.pallas_call(nested_kernel, out_shape=out)(projected)


def fsdp_sum(x):
    return lax.psum(lax.psum(x, "y"), "xl")


def pool_kernel(dp_shape, counts_ref, ids_ref, states_ref, squares_ref, out_ref):
    _, slots_n, _ = states_ref.shape
    spans = squares_ref.shape[0]
    z_n, xh_n, c_n = dp_shape
    sec_local = out_ref.shape[0] // (z_n * xh_n * c_n)
    me = (lax.axis_index("z") * xh_n + lax.axis_index("xh")) * c_n + lax.axis_index("c")
    c = pl.program_id(0)

    @pl.when(c == 0)
    def _():
        out_ref[...] = jnp.zeros(out_ref.shape, jnp.float32)

    rows = lax.broadcasted_iota(jnp.int32, (8, slots_n), 0)
    count = counts_ref[c]
    scale = lax.rsqrt(squares_ref[pl.ds(c, 1), :] / D + epsilon)
    slots = lax.broadcasted_iota(jnp.int32, scale.shape, 1)
    weights = jnp.where(slots < count, scale, 0.0)
    parts = jnp.where(rows < 3, split3(weights, rows), jnp.zeros((8, slots_n), jnp.bfloat16))
    partial = jnp.dot(parts, states_ref[0], preferred_element_type=jnp.float32)
    sums = partial[0:1, :] + partial[1:2, :] + partial[2:3, :]
    pooled = sums / count.astype(jnp.float32)
    section = ids_ref[me * spans + c]
    owner = section // sec_local
    place = ((owner % c_n) * xh_n + (owner // c_n) % xh_n) * z_n + owner // (c_n * xh_n)
    row = place * sec_local + section % sec_local
    out_ref[pl.ds(row, 1)] += pooled[None]


def split3(x, rows):
    high = x.astype(jnp.bfloat16)
    rest = x - high.astype(jnp.float32)
    middle = rest.astype(jnp.bfloat16)
    low = (rest - middle.astype(jnp.float32)).astype(jnp.bfloat16)
    return jnp.where(rows == 0, high, jnp.where(rows == 1, middle, low))


def split3_rounded(x):
    high = lax.reduce_precision(x, exponent_bits=8, mantissa_bits=7)
    rest = x - high
    middle = lax.reduce_precision(rest, exponent_bits=8, mantissa_bits=7)
    low = rest - middle
    return jnp.stack([high, middle, low]).astype(jnp.bfloat16)


def make_local(dp_shape):
    groups = dp_shape[0] * dp_shape[1] * dp_shape[2]

    def local(states, valid_counts, section_ids, norm_gain, head_weight):
        values = states.astype(jnp.float32)
        partial_squares = jnp.sum(values * values, axis=-1)
        squares = fsdp_sum(partial_squares)
        local_spans, slots_n, features = states.shape
        sec_local = local_spans // 2
        total_sections = sec_local * groups
        smem = pl.BlockSpec(memory_space=pltpu.SMEM)
        vmem = pl.BlockSpec(memory_space=pltpu.VMEM)
        contrib = pl.pallas_call(
            functools.partial(pool_kernel, dp_shape),
            out_shape=jax.ShapeDtypeStruct((total_sections, 1, features), jnp.float32),
            grid=(local_spans,),
            in_specs=[
                smem,
                smem,
                pl.BlockSpec((1, slots_n, features), lambda c: (c, 0, 0)),
                pl.BlockSpec((local_spans, slots_n), lambda c: (0, 0)),
            ],
            out_specs=pl.BlockSpec((total_sections, 1, features), lambda c: (0, 0, 0)),
        )(valid_counts, section_ids, states, squares)
        received = lax.all_to_all(contrib, ("c", "xh", "z"), 0, 0, tiled=True)
        section_sums = jnp.sum(received.reshape(groups, sec_local, features), axis=0)
        section_sums = section_sums * norm_gain.astype(jnp.float32)[None, :]
        parts = split3_rounded(section_sums)
        stacked = jnp.dot(parts.reshape(-1, features), head_weight, preferred_element_type=jnp.float32)
        terms = jnp.sum(stacked.reshape(3, sec_local, -1), axis=0)
        projected = fsdp_sum(terms)
        return nested(projected)

    return local


def solution(mesh):
    dp, fsdp = mesh.shape["dp"], mesh.shape["fsdp"]
    dp_shape = (dp // 4, 2, 2)
    fine = Mesh(mesh.devices.reshape(*dp_shape, 2, fsdp // 2), ("z", "xh", "c", "xl", "y"))
    spans = ("z", "xh", "c")
    features = ("xl", "y")
    in_specs = (P(spans, None, features), P(spans), P(), P(features), P(features, None))
    out_specs = P(spans, None)
    return jax.shard_map(make_local(dp_shape), mesh=fine, in_specs=in_specs, out_specs=out_specs, check_vma=False)
```

```python
import functools

import jax
import jax.numpy as jnp
from jax import lax
from jax.experimental import pallas as pl
from jax.experimental.pallas import tpu as pltpu
from jax.sharding import Mesh, PartitionSpec as P

D = 5120


epsilon = 1e-06


def nested_kernel(x_ref, o_ref):
    x = x_ref[...]
    width = x.shape[1]
    squared = x * x
    offset = 0
    for level in (width // 8, width // 4, width // 2, width):
        mean = jnp.sum(squared[:, :level], axis=1, keepdims=True) / level
        o_ref[:, offset:offset + level] = x[:, :level] * lax.rsqrt(mean + epsilon)
        offset += level


def nested(projected):
    rows, width = projected.shape
    out = jax.ShapeDtypeStruct((rows, width // 8 + width // 4 + width // 2 + width), jnp.float32)
    vmem = pl.BlockSpec(memory_space=pltpu.VMEM)
    return pl.pallas_call(nested_kernel, out_shape=out, in_specs=[vmem])(
        pltpu.with_memory_space_constraint(projected, pltpu.VMEM)
    )


def fsdp_sum(x):
    return lax.psum(lax.psum(x, "y"), "xl")


def pool_kernel(dp_shape, counts_ref, ids_ref, states_ref, squares_ref, out_ref):
    _, slots_n, _ = states_ref.shape
    spans = squares_ref.shape[0]
    z_n, xh_n, c_n = dp_shape
    sec_local = out_ref.shape[0] // (z_n * xh_n * c_n)
    me = (lax.axis_index("z") * xh_n + lax.axis_index("xh")) * c_n + lax.axis_index("c")
    c = pl.program_id(0)

    @pl.when(c == 0)
    def _():
        out_ref[...] = jnp.zeros(out_ref.shape, jnp.float32)

    rows = lax.broadcasted_iota(jnp.int32, (8, slots_n), 0)
    count = counts_ref[c]
    scale = lax.rsqrt(squares_ref[pl.ds(c, 1), :] / D + epsilon)
    slots = lax.broadcasted_iota(jnp.int32, scale.shape, 1)
    weights = jnp.where(slots < count, scale, 0.0)
    parts = jnp.where(rows < 3, split3(weights, rows), jnp.zeros((8, slots_n), jnp.bfloat16))
    partial = jnp.dot(parts, states_ref[0], preferred_element_type=jnp.float32)
    sums = partial[0:1, :] + partial[1:2, :] + partial[2:3, :]
    pooled = sums / count.astype(jnp.float32)
    section = ids_ref[me * spans + c]
    owner = section // sec_local
    place = ((owner % c_n) * xh_n + (owner // c_n) % xh_n) * z_n + owner // (c_n * xh_n)
    row = place * sec_local + section % sec_local
    out_ref[pl.ds(row, 1)] += pooled[None]


def split3(x, rows):
    high = x.astype(jnp.bfloat16)
    rest = x - high.astype(jnp.float32)
    middle = rest.astype(jnp.bfloat16)
    low = (rest - middle.astype(jnp.float32)).astype(jnp.bfloat16)
    return jnp.where(rows == 0, high, jnp.where(rows == 1, middle, low))


def split3_rounded(x):
    high = lax.reduce_precision(x, exponent_bits=8, mantissa_bits=7)
    rest = x - high
    middle = lax.reduce_precision(rest, exponent_bits=8, mantissa_bits=7)
    low = rest - middle
    return jnp.stack([high, middle, low]).astype(jnp.bfloat16)


def make_local(dp_shape):
    groups = dp_shape[0] * dp_shape[1] * dp_shape[2]

    def local(states, valid_counts, section_ids, norm_gain, head_weight):
        values = states.astype(jnp.float32)
        partial_squares = jnp.sum(values * values, axis=-1)
        squares = fsdp_sum(partial_squares)
        local_spans, slots_n, features = states.shape
        sec_local = local_spans // 2
        total_sections = sec_local * groups
        smem = pl.BlockSpec(memory_space=pltpu.SMEM)
        vmem = pl.BlockSpec(memory_space=pltpu.VMEM)
        contrib = pl.pallas_call(
            functools.partial(pool_kernel, dp_shape),
            out_shape=jax.ShapeDtypeStruct((total_sections, 1, features), jnp.float32),
            grid=(local_spans,),
            in_specs=[
                smem,
                smem,
                pl.BlockSpec((1, slots_n, features), lambda c: (c, 0, 0)),
                pl.BlockSpec((local_spans, slots_n), lambda c: (0, 0), memory_space=pltpu.VMEM),
            ],
            out_specs=pl.BlockSpec((total_sections, 1, features), lambda c: (0, 0, 0)),
        )(valid_counts, section_ids, states, pltpu.with_memory_space_constraint(squares, pltpu.VMEM))
        received = lax.all_to_all(contrib, ("c", "xh", "z"), 0, 0, tiled=True)
        section_sums = jnp.sum(received.reshape(groups, sec_local, features), axis=0)
        section_sums = section_sums * norm_gain.astype(jnp.float32)[None, :]
        parts = split3_rounded(section_sums)
        stacked = jnp.dot(parts.reshape(-1, features), head_weight, preferred_element_type=jnp.float32)
        terms = jnp.sum(stacked.reshape(3, sec_local, -1), axis=0)
        projected = fsdp_sum(terms)
        return nested(projected)

    return local


def solution(mesh):
    dp, fsdp = mesh.shape["dp"], mesh.shape["fsdp"]
    dp_shape = (dp // 4, 2, 2)
    fine = Mesh(mesh.devices.reshape(*dp_shape, 2, fsdp // 2), ("z", "xh", "c", "xl", "y"))
    spans = ("z", "xh", "c")
    features = ("xl", "y")
    in_specs = (P(spans, None, features), P(spans), P(), P(features), P(features, None))
    out_specs = P(spans, None)
    return jax.shard_map(make_local(dp_shape), mesh=fine, in_specs=in_specs, out_specs=out_specs, check_vma=False)
```

```python
import functools

import jax
import jax.numpy as jnp
from jax import lax
from jax.experimental import pallas as pl
from jax.experimental.pallas import tpu as pltpu
from jax.sharding import Mesh, PartitionSpec as P

D = 5120


epsilon = 1e-06


def nested_kernel(x_ref, o_ref):
    x = x_ref[...]
    width = x.shape[1]
    squared = x * x
    offset = 0
    for level in (width // 8, width // 4, width // 2, width):
        mean = jnp.sum(squared[:, :level], axis=1, keepdims=True) / level
        o_ref[:, offset:offset + level] = x[:, :level] * lax.rsqrt(mean + epsilon)
        offset += level


def nested(projected):
    rows, width = projected.shape
    out = jax.ShapeDtypeStruct((rows, width // 8 + width // 4 + width // 2 + width), jnp.float32)
    vmem = pl.BlockSpec(memory_space=pltpu.VMEM)
    return pl.pallas_call(nested_kernel, out_shape=out, in_specs=[vmem])(
        pltpu.with_memory_space_constraint(projected, pltpu.VMEM)
    )


def fsdp_sum(x):
    return lax.psum(lax.psum(x, "y"), "xl")


def pool_kernel(dp_shape, counts_ref, ids_ref, states_ref, squares_ref, out_ref):
    _, slots_n, _ = states_ref.shape
    spans = squares_ref.shape[0]
    z_n, xh_n, c_n = dp_shape
    sec_local = out_ref.shape[0] // (z_n * xh_n * c_n)
    me = (lax.axis_index("z") * xh_n + lax.axis_index("xh")) * c_n + lax.axis_index("c")
    c = pl.program_id(0)

    @pl.when(c == 0)
    def _():
        out_ref[...] = jnp.zeros(out_ref.shape, jnp.float32)

    rows = lax.broadcasted_iota(jnp.int32, (8, slots_n), 0)
    count = counts_ref[c]
    scale = lax.rsqrt(squares_ref[pl.ds(c, 1), :] / D + epsilon)
    slots = lax.broadcasted_iota(jnp.int32, scale.shape, 1)
    weights = jnp.where(slots < count, scale, 0.0)
    parts = jnp.where(rows < 3, split3(weights, rows), jnp.zeros((8, slots_n), jnp.bfloat16))
    partial = jnp.dot(parts, states_ref[0], preferred_element_type=jnp.float32)
    sums = partial[0:1, :] + partial[1:2, :] + partial[2:3, :]
    pooled = sums / count.astype(jnp.float32)
    section = ids_ref[me * spans + c]
    owner = section // sec_local
    place = ((owner % c_n) * xh_n + (owner // c_n) % xh_n) * z_n + owner // (c_n * xh_n)
    row = place * sec_local + section % sec_local
    out_ref[pl.ds(row, 1)] += pooled[None]


def split3(x, rows):
    high = x.astype(jnp.bfloat16)
    rest = x - high.astype(jnp.float32)
    middle = rest.astype(jnp.bfloat16)
    low = (rest - middle.astype(jnp.float32)).astype(jnp.bfloat16)
    return jnp.where(rows == 0, high, jnp.where(rows == 1, middle, low))


def split3_rounded(x):
    high = lax.reduce_precision(x, exponent_bits=8, mantissa_bits=7)
    rest = x - high
    middle = lax.reduce_precision(rest, exponent_bits=8, mantissa_bits=7)
    low = rest - middle
    return jnp.stack([high, middle, low]).astype(jnp.bfloat16)


def make_local(dp_shape):
    groups = dp_shape[0] * dp_shape[1] * dp_shape[2]

    def local(states, valid_counts, section_ids, norm_gain, head_weight):
        values = states.astype(jnp.float32)
        partial_squares = jnp.sum(values * values, axis=-1)
        squares = fsdp_sum(partial_squares)
        local_spans, slots_n, features = states.shape
        sec_local = local_spans // 2
        total_sections = sec_local * groups
        smem = pl.BlockSpec(memory_space=pltpu.SMEM)
        vmem = pl.BlockSpec(memory_space=pltpu.VMEM)
        contrib = pl.pallas_call(
            functools.partial(pool_kernel, dp_shape),
            out_shape=pltpu.VMEM((total_sections, 1, features), jnp.float32),
            grid=(local_spans,),
            in_specs=[
                smem,
                smem,
                pl.BlockSpec((1, slots_n, features), lambda c: (c, 0, 0)),
                pl.BlockSpec((local_spans, slots_n), lambda c: (0, 0), memory_space=pltpu.VMEM),
            ],
            out_specs=pl.BlockSpec((total_sections, 1, features), lambda c: (0, 0, 0), memory_space=pltpu.VMEM),
        )(valid_counts, section_ids, states, pltpu.with_memory_space_constraint(squares, pltpu.VMEM))
        received = lax.all_to_all(contrib, ("c", "xh", "z"), 0, 0, tiled=True)
        section_sums = jnp.sum(received.reshape(groups, sec_local, features), axis=0)
        section_sums = section_sums * norm_gain.astype(jnp.float32)[None, :]
        parts = split3_rounded(section_sums)
        stacked = jnp.dot(parts.reshape(-1, features), head_weight, preferred_element_type=jnp.float32)
        terms = jnp.sum(stacked.reshape(3, sec_local, -1), axis=0)
        projected = fsdp_sum(terms)
        return nested(projected)

    return local


def solution(mesh):
    dp, fsdp = mesh.shape["dp"], mesh.shape["fsdp"]
    dp_shape = (dp // 4, 2, 2)
    fine = Mesh(mesh.devices.reshape(*dp_shape, 2, fsdp // 2), ("z", "xh", "c", "xl", "y"))
    spans = ("z", "xh", "c")
    features = ("xl", "y")
    in_specs = (P(spans, None, features), P(spans), P(), P(features), P(features, None))
    out_specs = P(spans, None)
    return jax.shard_map(make_local(dp_shape), mesh=fine, in_specs=in_specs, out_specs=out_specs, check_vma=False)
```

```python
import functools

import jax
import jax.numpy as jnp
from jax import lax
from jax.experimental import pallas as pl
from jax.experimental.pallas import tpu as pltpu
from jax.sharding import Mesh, PartitionSpec as P

D = 5120


epsilon = 1e-06


def nested_kernel(x_ref, o_ref):
    x = x_ref[...]
    width = x.shape[1]
    squared = x * x
    offset = 0
    for level in (width // 8, width // 4, width // 2, width):
        mean = jnp.sum(squared[:, :level], axis=1, keepdims=True) / level
        o_ref[:, offset:offset + level] = x[:, :level] * lax.rsqrt(mean + epsilon)
        offset += level


def nested(projected):
    rows, width = projected.shape
    out = jax.ShapeDtypeStruct((rows, width // 8 + width // 4 + width // 2 + width), jnp.float32)
    vmem = pl.BlockSpec(memory_space=pltpu.VMEM)
    return pl.pallas_call(nested_kernel, out_shape=out, in_specs=[vmem])(
        pltpu.with_memory_space_constraint(projected, pltpu.VMEM)
    )


def fsdp_sum(x):
    return lax.psum(lax.psum(x, "y"), "xl")


def pool_kernel(dp_shape, counts_ref, ids_ref, states_ref, squares_ref, out_ref):
    spans, slots_n, _ = states_ref.shape
    z_n, xh_n, c_n = dp_shape
    sec_local = out_ref.shape[0] // (z_n * xh_n * c_n)
    me = (lax.axis_index("z") * xh_n + lax.axis_index("xh")) * c_n + lax.axis_index("c")
    out_ref[...] = jnp.zeros(out_ref.shape, jnp.float32)
    rows = lax.broadcasted_iota(jnp.int32, (8, slots_n), 0)
    for c in range(spans):
        count = counts_ref[c]
        scale = lax.rsqrt(squares_ref[pl.ds(c, 1), :] / D + epsilon)
        slots = lax.broadcasted_iota(jnp.int32, scale.shape, 1)
        weights = jnp.where(slots < count, scale, 0.0)
        parts = jnp.where(rows < 3, split3(weights, rows), jnp.zeros((8, slots_n), jnp.bfloat16))
        partial = jnp.dot(parts, states_ref[c], preferred_element_type=jnp.float32)
        sums = partial[0:1, :] + partial[1:2, :] + partial[2:3, :]
        pooled = sums / count.astype(jnp.float32)
        section = ids_ref[me * spans + c]
        owner = section // sec_local
        place = ((owner % c_n) * xh_n + (owner // c_n) % xh_n) * z_n + owner // (c_n * xh_n)
        row = place * sec_local + section % sec_local
        out_ref[pl.ds(row, 1)] += pooled[None]


def split3(x, rows):
    high = x.astype(jnp.bfloat16)
    rest = x - high.astype(jnp.float32)
    middle = rest.astype(jnp.bfloat16)
    low = (rest - middle.astype(jnp.float32)).astype(jnp.bfloat16)
    return jnp.where(rows == 0, high, jnp.where(rows == 1, middle, low))


def split3_rounded(x):
    high = lax.reduce_precision(x, exponent_bits=8, mantissa_bits=7)
    rest = x - high
    middle = lax.reduce_precision(rest, exponent_bits=8, mantissa_bits=7)
    low = rest - middle
    return jnp.stack([high, middle, low]).astype(jnp.bfloat16)


def squares_kernel(states_ref, squares_ref, copy_ref):
    spans, slots_n, _ = states_ref.shape
    for c in range(spans):
        values = states_ref[c]
        copy_ref[c] = values
        wide = values.astype(jnp.float32)
        column = jnp.sum(wide * wide, axis=1, keepdims=True)
        squares_ref[pl.ds(c, 1), :] = jnp.transpose(jnp.broadcast_to(column, (slots_n, 128)))[:1, :]


def make_local(dp_shape):
    groups = dp_shape[0] * dp_shape[1] * dp_shape[2]

    def local(states, valid_counts, section_ids, norm_gain, head_weight):
        local_spans, slots_n, features = states.shape
        vmem = pl.BlockSpec(memory_space=pltpu.VMEM)
        partial_squares, resident = pl.pallas_call(
            squares_kernel,
            out_shape=(pltpu.VMEM((local_spans, slots_n), jnp.float32), pltpu.VMEM(states.shape, states.dtype)),
            out_specs=(vmem, vmem),
        )(states)
        squares = fsdp_sum(partial_squares)
        sec_local = local_spans // 2
        total_sections = sec_local * groups
        smem = pl.BlockSpec(memory_space=pltpu.SMEM)
        vmem = pl.BlockSpec(memory_space=pltpu.VMEM)
        contrib = pl.pallas_call(
            functools.partial(pool_kernel, dp_shape),
            out_shape=pltpu.VMEM((total_sections, 1, features), jnp.float32),
            in_specs=[smem, smem, vmem, vmem],
            out_specs=vmem,
        )(
            valid_counts,
            section_ids,
            pltpu.with_memory_space_constraint(resident, pltpu.VMEM),
            pltpu.with_memory_space_constraint(squares, pltpu.VMEM),
        )
        received = lax.all_to_all(contrib, ("c", "xh", "z"), 0, 0, tiled=True)
        section_sums = jnp.sum(received.reshape(groups, sec_local, features), axis=0)
        section_sums = section_sums * norm_gain.astype(jnp.float32)[None, :]
        parts = split3_rounded(section_sums)
        stacked = jnp.dot(parts.reshape(-1, features), head_weight, preferred_element_type=jnp.float32)
        terms = jnp.sum(stacked.reshape(3, sec_local, -1), axis=0)
        projected = fsdp_sum(terms)
        return nested(projected)

    return local


def solution(mesh):
    dp, fsdp = mesh.shape["dp"], mesh.shape["fsdp"]
    dp_shape = (dp // 4, 2, 2)
    fine = Mesh(mesh.devices.reshape(*dp_shape, 2, fsdp // 2), ("z", "xh", "c", "xl", "y"))
    spans = ("z", "xh", "c")
    features = ("xl", "y")
    in_specs = (P(spans, None, features), P(spans), P(), P(features), P(features, None))
    out_specs = P(spans, None)
    return jax.shard_map(make_local(dp_shape), mesh=fine, in_specs=in_specs, out_specs=out_specs, check_vma=False)
```

```python
import functools

import jax
import jax.numpy as jnp
from jax import lax
from jax.experimental import pallas as pl
from jax.experimental.pallas import tpu as pltpu
from jax.sharding import Mesh, PartitionSpec as P

D = 5120


epsilon = 1e-06


def nested_kernel(x_ref, o_ref):
    x = x_ref[...]
    width = x.shape[1]
    squared = x * x
    offset = 0
    for level in (width // 8, width // 4, width // 2, width):
        mean = jnp.sum(squared[:, :level], axis=1, keepdims=True) / level
        o_ref[:, offset:offset + level] = x[:, :level] * lax.rsqrt(mean + epsilon)
        offset += level


def nested(projected):
    rows, width = projected.shape
    out = jax.ShapeDtypeStruct((rows, width // 8 + width // 4 + width // 2 + width), jnp.float32)
    vmem = pl.BlockSpec(memory_space=pltpu.VMEM)
    return pl.pallas_call(nested_kernel, out_shape=out, in_specs=[vmem])(
        pltpu.with_memory_space_constraint(projected, pltpu.VMEM)
    )


def fsdp_sum(x):
    return lax.psum(lax.psum(x, "y"), "xl")


def pool_kernel(dp_shape, counts_ref, ids_ref, states_ref, squares_ref, out_ref, acc_ref):
    _, piece, _ = states_ref.shape
    spans = squares_ref.shape[0]
    z_n, xh_n, c_n = dp_shape
    sec_local = out_ref.shape[0] // (z_n * xh_n * c_n)
    me = (lax.axis_index("z") * xh_n + lax.axis_index("xh")) * c_n + lax.axis_index("c")
    c = pl.program_id(0)
    h = pl.program_id(1)
    last = pl.num_programs(1) - 1

    @pl.when((c == 0) & (h == 0))
    def _():
        out_ref[...] = jnp.zeros(out_ref.shape, jnp.float32)

    rows = lax.broadcasted_iota(jnp.int32, (8, piece), 0)
    count = counts_ref[c]
    start = pl.multiple_of(h * piece, piece)
    scale = lax.rsqrt(squares_ref[pl.ds(c, 1), pl.ds(start, piece)] / D + epsilon)
    slots = lax.broadcasted_iota(jnp.int32, scale.shape, 1) + start
    weights = jnp.where(slots < count, scale, 0.0)
    parts = jnp.where(rows < 3, split3(weights, rows), jnp.zeros((8, piece), jnp.bfloat16))
    partial = jnp.dot(parts, states_ref[0], preferred_element_type=jnp.float32)

    @pl.when(h == 0)
    def _():
        acc_ref[...] = partial

    @pl.when(h > 0)
    def _():
        acc_ref[...] += partial

    @pl.when(h == last)
    def _():
        total = acc_ref[...]
        sums = total[0:1, :] + total[1:2, :] + total[2:3, :]
        pooled = sums / count.astype(jnp.float32)
        section = ids_ref[me * spans + c]
        owner = section // sec_local
        place = ((owner % c_n) * xh_n + (owner // c_n) % xh_n) * z_n + owner // (c_n * xh_n)
        row = place * sec_local + section % sec_local
        out_ref[pl.ds(row, 1)] += pooled[None]


def split3(x, rows):
    high = x.astype(jnp.bfloat16)
    rest = x - high.astype(jnp.float32)
    middle = rest.astype(jnp.bfloat16)
    low = (rest - middle.astype(jnp.float32)).astype(jnp.bfloat16)
    return jnp.where(rows == 0, high, jnp.where(rows == 1, middle, low))


def split3_rounded(x):
    high = lax.reduce_precision(x, exponent_bits=8, mantissa_bits=7)
    rest = x - high
    middle = lax.reduce_precision(rest, exponent_bits=8, mantissa_bits=7)
    low = rest - middle
    return jnp.stack([high, middle, low]).astype(jnp.bfloat16)


def make_local(dp_shape):
    groups = dp_shape[0] * dp_shape[1] * dp_shape[2]

    def local(states, valid_counts, section_ids, norm_gain, head_weight):
        values = states.astype(jnp.float32)
        partial_squares = jnp.sum(values * values, axis=-1)
        squares = fsdp_sum(partial_squares)
        local_spans, slots_n, features = states.shape
        sec_local = local_spans // 2
        total_sections = sec_local * groups
        smem = pl.BlockSpec(memory_space=pltpu.SMEM)
        vmem = pl.BlockSpec(memory_space=pltpu.VMEM)
        contrib = pl.pallas_call(
            functools.partial(pool_kernel, dp_shape),
            out_shape=pltpu.VMEM((total_sections, 1, features), jnp.float32),
            grid=(local_spans, 2),
            in_specs=[
                smem,
                smem,
                pl.BlockSpec((1, slots_n // 2, features), lambda c, h: (c, h, 0)),
                pl.BlockSpec((local_spans, slots_n), lambda c, h: (0, 0), memory_space=pltpu.VMEM),
            ],
            out_specs=pl.BlockSpec((total_sections, 1, features), lambda c, h: (0, 0, 0), memory_space=pltpu.VMEM),
            scratch_shapes=[pltpu.VMEM((8, features), jnp.float32)],
        )(valid_counts, section_ids, states, pltpu.with_memory_space_constraint(squares, pltpu.VMEM))
        received = lax.all_to_all(contrib, ("c", "xh", "z"), 0, 0, tiled=True)
        section_sums = jnp.sum(received.reshape(groups, sec_local, features), axis=0)
        section_sums = section_sums * norm_gain.astype(jnp.float32)[None, :]
        parts = split3_rounded(section_sums)
        stacked = jnp.dot(parts.reshape(-1, features), head_weight, preferred_element_type=jnp.float32)
        terms = jnp.sum(stacked.reshape(3, sec_local, -1), axis=0)
        projected = fsdp_sum(terms)
        return nested(projected)

    return local


def solution(mesh):
    dp, fsdp = mesh.shape["dp"], mesh.shape["fsdp"]
    dp_shape = (dp // 4, 2, 2)
    fine = Mesh(mesh.devices.reshape(*dp_shape, 2, fsdp // 2), ("z", "xh", "c", "xl", "y"))
    spans = ("z", "xh", "c")
    features = ("xl", "y")
    in_specs = (P(spans, None, features), P(spans), P(), P(features), P(features, None))
    out_specs = P(spans, None)
    return jax.shard_map(make_local(dp_shape), mesh=fine, in_specs=in_specs, out_specs=out_specs, check_vma=False)
```

```python
import functools

import jax
import jax.numpy as jnp
from jax import lax
from jax.experimental import pallas as pl
from jax.experimental.pallas import tpu as pltpu
from jax.sharding import Mesh, PartitionSpec as P

D = 5120


epsilon = 1e-06


def nested_kernel(x_ref, o_ref):
    x = x_ref[...]
    width = x.shape[1]
    squared = x * x
    offset = 0
    for level in (width // 8, width // 4, width // 2, width):
        mean = jnp.sum(squared[:, :level], axis=1, keepdims=True) / level
        o_ref[:, offset:offset + level] = x[:, :level] * lax.rsqrt(mean + epsilon)
        offset += level


def nested(projected):
    rows, width = projected.shape
    out = jax.ShapeDtypeStruct((rows, width // 8 + width // 4 + width // 2 + width), jnp.float32)
    vmem = pl.BlockSpec(memory_space=pltpu.VMEM)
    return pl.pallas_call(nested_kernel, out_shape=out, in_specs=[vmem])(
        pltpu.with_memory_space_constraint(projected, pltpu.VMEM)
    )


def fsdp_sum(x):
    return lax.psum(lax.psum(x, "y"), "xl")


def pool_kernel(dp_shape, counts_ref, ids_ref, states_ref, squares_ref, out_ref):
    spans, slots_n, _ = states_ref.shape
    z_n, xh_n, c_n = dp_shape
    sec_local = out_ref.shape[0] // (z_n * xh_n * c_n)
    me = (lax.axis_index("z") * xh_n + lax.axis_index("xh")) * c_n + lax.axis_index("c")
    out_ref[...] = jnp.zeros(out_ref.shape, jnp.float32)
    rows = lax.broadcasted_iota(jnp.int32, (8, slots_n), 0)
    for c in range(spans):
        count = counts_ref[c]
        scale = lax.rsqrt(squares_ref[pl.ds(c, 1), :] / D + epsilon)
        slots = lax.broadcasted_iota(jnp.int32, scale.shape, 1)
        weights = jnp.where(slots < count, scale, 0.0)
        parts = jnp.where(rows < 3, split3(weights, rows), jnp.zeros((8, slots_n), jnp.bfloat16))
        partial = jnp.dot(parts, states_ref[c], preferred_element_type=jnp.float32)
        sums = partial[0:1, :] + partial[1:2, :] + partial[2:3, :]
        pooled = sums / count.astype(jnp.float32)
        section = ids_ref[me * spans + c]
        owner = section // sec_local
        place = ((owner % c_n) * xh_n + (owner // c_n) % xh_n) * z_n + owner // (c_n * xh_n)
        row = place * sec_local + section % sec_local
        out_ref[pl.ds(row, 1)] += pooled[None]


def split3(x, rows):
    high = x.astype(jnp.bfloat16)
    rest = x - high.astype(jnp.float32)
    middle = rest.astype(jnp.bfloat16)
    low = (rest - middle.astype(jnp.float32)).astype(jnp.bfloat16)
    return jnp.where(rows == 0, high, jnp.where(rows == 1, middle, low))


def split3_rounded(x):
    high = lax.reduce_precision(x, exponent_bits=8, mantissa_bits=7)
    rest = x - high
    middle = lax.reduce_precision(rest, exponent_bits=8, mantissa_bits=7)
    low = rest - middle
    return jnp.stack([high, middle, low]).astype(jnp.bfloat16)


def make_local(dp_shape):
    groups = dp_shape[0] * dp_shape[1] * dp_shape[2]

    def local(states, valid_counts, section_ids, norm_gain, head_weight):
        values = states.astype(jnp.float32)
        partial_squares = jnp.sum(values * values, axis=-1)
        squares = fsdp_sum(partial_squares)
        local_spans, slots_n, features = states.shape
        sec_local = local_spans // 2
        total_sections = sec_local * groups
        smem = pl.BlockSpec(memory_space=pltpu.SMEM)
        vmem = pl.BlockSpec(memory_space=pltpu.VMEM)
        contrib = pl.pallas_call(
            functools.partial(pool_kernel, dp_shape),
            out_shape=pltpu.VMEM((total_sections, 1, features), jnp.float32),
            in_specs=[smem, smem, vmem, vmem],
            out_specs=vmem,
        )(valid_counts, section_ids, states, pltpu.with_memory_space_constraint(squares, pltpu.VMEM))
        received = lax.all_to_all(contrib, ("c", "xh", "z"), 0, 0, tiled=True)
        section_sums = jnp.sum(received.reshape(groups, sec_local, features), axis=0)
        section_sums = section_sums * norm_gain.astype(jnp.float32)[None, :]
        parts = split3_rounded(section_sums)
        stacked = jnp.dot(parts.reshape(-1, features), head_weight, preferred_element_type=jnp.float32)
        terms = jnp.sum(stacked.reshape(3, sec_local, -1), axis=0)
        projected = fsdp_sum(terms)
        return nested(projected)

    return local


def solution(mesh):
    dp, fsdp = mesh.shape["dp"], mesh.shape["fsdp"]
    dp_shape = (dp // 4, 2, 2)
    fine = Mesh(mesh.devices.reshape(*dp_shape, 2, fsdp // 2), ("z", "xh", "c", "xl", "y"))
    spans = ("z", "xh", "c")
    features = ("xl", "y")
    in_specs = (P(spans, None, features), P(spans), P(), P(features), P(features, None))
    out_specs = P(spans, None)
    return jax.shard_map(make_local(dp_shape), mesh=fine, in_specs=in_specs, out_specs=out_specs, check_vma=False)
```

```python
import functools

import jax
import jax.numpy as jnp
from jax import lax
from jax.experimental import pallas as pl
from jax.experimental.pallas import tpu as pltpu
from jax.sharding import Mesh, PartitionSpec as P

D = 5120


epsilon = 1e-06


def nested_kernel(x_ref, o_ref):
    x = x_ref[...]
    width = x.shape[1]
    squared = x * x
    offset = 0
    for level in (width // 8, width // 4, width // 2, width):
        mean = jnp.sum(squared[:, :level], axis=1, keepdims=True) / level
        o_ref[:, offset:offset + level] = x[:, :level] * lax.rsqrt(mean + epsilon)
        offset += level


def nested(projected):
    rows, width = projected.shape
    out = jax.ShapeDtypeStruct((rows, width // 8 + width // 4 + width // 2 + width), jnp.float32)
    vmem = pl.BlockSpec(memory_space=pltpu.VMEM)
    return pl.pallas_call(nested_kernel, out_shape=out, in_specs=[vmem])(
        pltpu.with_memory_space_constraint(projected, pltpu.VMEM)
    )


def fsdp_sum(x):
    return lax.psum(lax.psum(x, "y"), "xl")


def pool_kernel(dp_shape, counts_ref, ids_ref, states_ref, squares_ref, out_ref):
    _, slots_n, _ = states_ref.shape
    spans = squares_ref.shape[0]
    z_n, xh_n, c_n = dp_shape
    sec_local = out_ref.shape[0] // (z_n * xh_n * c_n)
    me = (lax.axis_index("z") * xh_n + lax.axis_index("xh")) * c_n + lax.axis_index("c")
    c = pl.program_id(0)

    @pl.when(c == 0)
    def _():
        out_ref[...] = jnp.zeros(out_ref.shape, jnp.float32)

    rows = lax.broadcasted_iota(jnp.int32, (8, slots_n), 0)
    count = counts_ref[c]
    scale = lax.rsqrt(squares_ref[pl.ds(c, 1), :] / D + epsilon)
    slots = lax.broadcasted_iota(jnp.int32, scale.shape, 1)
    weights = jnp.where(slots < count, scale, 0.0)
    parts = jnp.where(rows < 3, split3(weights, rows), jnp.zeros((8, slots_n), jnp.bfloat16))
    partial = jnp.dot(parts, states_ref[0], preferred_element_type=jnp.float32)
    sums = partial[0:1, :] + partial[1:2, :] + partial[2:3, :]
    pooled = sums / count.astype(jnp.float32)
    section = ids_ref[me * spans + c]
    owner = section // sec_local
    place = ((owner % c_n) * xh_n + (owner // c_n) % xh_n) * z_n + owner // (c_n * xh_n)
    row = place * sec_local + section % sec_local
    out_ref[pl.ds(row, 1)] += pooled[None]


def split3(x, rows):
    high = x.astype(jnp.bfloat16)
    rest = x - high.astype(jnp.float32)
    middle = rest.astype(jnp.bfloat16)
    low = (rest - middle.astype(jnp.float32)).astype(jnp.bfloat16)
    return jnp.where(rows == 0, high, jnp.where(rows == 1, middle, low))


def split3_rounded(x):
    high = lax.reduce_precision(x, exponent_bits=8, mantissa_bits=7)
    rest = x - high
    middle = lax.reduce_precision(rest, exponent_bits=8, mantissa_bits=7)
    low = rest - middle
    return jnp.stack([high, middle, low]).astype(jnp.bfloat16)


def make_local(dp_shape):
    groups = dp_shape[0] * dp_shape[1] * dp_shape[2]

    def local(states, valid_counts, section_ids, norm_gain, head_weight):
        values = states.astype(jnp.float32)
        partial_squares = jnp.sum(values * values, axis=-1)
        squares = fsdp_sum(partial_squares)
        local_spans, slots_n, features = states.shape
        sec_local = local_spans // 2
        total_sections = sec_local * groups
        smem = pl.BlockSpec(memory_space=pltpu.SMEM)
        vmem = pl.BlockSpec(memory_space=pltpu.VMEM)
        contrib = pl.pallas_call(
            functools.partial(pool_kernel, dp_shape),
            out_shape=pltpu.VMEM((total_sections, 1, features), jnp.float32),
            grid=(local_spans,),
            in_specs=[
                smem,
                smem,
                pl.BlockSpec((1, slots_n, features), lambda c: (c, 0, 0)),
                pl.BlockSpec((local_spans, slots_n), lambda c: (0, 0), memory_space=pltpu.VMEM),
            ],
            out_specs=pl.BlockSpec((total_sections, 1, features), lambda c: (0, 0, 0), memory_space=pltpu.VMEM),
        )(valid_counts, section_ids, states, pltpu.with_memory_space_constraint(squares, pltpu.VMEM))
        received = lax.all_to_all(contrib, ("c", "xh", "z"), 0, 0, tiled=True)
        section_sums = jnp.sum(received.reshape(groups, sec_local, features), axis=0)
        section_sums = section_sums * norm_gain.astype(jnp.float32)[None, :]
        parts = split3_rounded(section_sums)
        stacked = jnp.dot(parts.reshape(-1, features), head_weight, preferred_element_type=jnp.float32)
        terms = jnp.sum(stacked.reshape(3, sec_local, -1), axis=0)
        projected = fsdp_sum(terms.reshape(-1, 128)).reshape(terms.shape)
        return nested(projected)

    return local


def solution(mesh):
    dp, fsdp = mesh.shape["dp"], mesh.shape["fsdp"]
    dp_shape = (dp // 4, 2, 2)
    fine = Mesh(mesh.devices.reshape(*dp_shape, 2, fsdp // 2), ("z", "xh", "c", "xl", "y"))
    spans = ("z", "xh", "c")
    features = ("xl", "y")
    in_specs = (P(spans, None, features), P(spans), P(), P(features), P(features, None))
    out_specs = P(spans, None)
    return jax.shard_map(make_local(dp_shape), mesh=fine, in_specs=in_specs, out_specs=out_specs, check_vma=False)
```

```python
import functools

import jax
import jax.numpy as jnp
from jax import lax
from jax.experimental import pallas as pl
from jax.experimental.pallas import tpu as pltpu
from jax.sharding import Mesh, PartitionSpec as P

D = 5120


epsilon = 1e-06


def nested_kernel(x_ref, o_ref):
    x = x_ref[...]
    width = x.shape[1]
    squared = x * x
    offset = 0
    for level in (width // 8, width // 4, width // 2, width):
        mean = jnp.sum(squared[:, :level], axis=1, keepdims=True) / level
        o_ref[:, offset:offset + level] = x[:, :level] * lax.rsqrt(mean + epsilon)
        offset += level


def nested(projected):
    rows, width = projected.shape
    out = jax.ShapeDtypeStruct((rows, width // 8 + width // 4 + width // 2 + width), jnp.float32)
    vmem = pl.BlockSpec(memory_space=pltpu.VMEM)
    return pl.pallas_call(nested_kernel, out_shape=out, in_specs=[vmem])(
        pltpu.with_memory_space_constraint(projected, pltpu.VMEM)
    )


def fsdp_sum(x):
    return lax.psum(lax.psum(x, "y"), "xl")


def pool_kernel(dp_shape, counts_ref, ids_ref, states_ref, squares_ref, out_ref):
    _, slots_n, _ = states_ref.shape
    spans = squares_ref.shape[0]
    z_n, xh_n, c_n = dp_shape
    sec_local = out_ref.shape[0] // (z_n * xh_n * c_n)
    me = (lax.axis_index("z") * xh_n + lax.axis_index("xh")) * c_n + lax.axis_index("c")
    c = pl.program_id(0)

    @pl.when(c == 0)
    def _():
        out_ref[...] = jnp.zeros(out_ref.shape, jnp.float32)

    rows = lax.broadcasted_iota(jnp.int32, (8, slots_n), 0)
    count = counts_ref[c]
    scale = lax.rsqrt(squares_ref[pl.ds(c, 1), :] / D + epsilon)
    slots = lax.broadcasted_iota(jnp.int32, scale.shape, 1)
    weights = jnp.where(slots < count, scale, 0.0)
    parts = jnp.where(rows < 3, split3(weights, rows), jnp.zeros((8, slots_n), jnp.bfloat16))
    partial = jnp.dot(parts, states_ref[0], preferred_element_type=jnp.float32)
    sums = partial[0:1, :] + partial[1:2, :] + partial[2:3, :]
    pooled = sums / count.astype(jnp.float32)
    section = ids_ref[me * spans + c]
    owner = section // sec_local
    place = ((owner % c_n) * xh_n + (owner // c_n) % xh_n) * z_n + owner // (c_n * xh_n)
    row = place * sec_local + section % sec_local
    out_ref[pl.ds(row, 1)] += pooled[None]


def split3(x, rows):
    high = x.astype(jnp.bfloat16)
    rest = x - high.astype(jnp.float32)
    middle = rest.astype(jnp.bfloat16)
    low = (rest - middle.astype(jnp.float32)).astype(jnp.bfloat16)
    return jnp.where(rows == 0, high, jnp.where(rows == 1, middle, low))


def split3_rounded(x):
    high = lax.reduce_precision(x, exponent_bits=8, mantissa_bits=7)
    rest = x - high
    middle = lax.reduce_precision(rest, exponent_bits=8, mantissa_bits=7)
    low = rest - middle
    return jnp.stack([high, middle, low]).astype(jnp.bfloat16)


def squares_kernel(states_ref, squares_ref):
    spans, slots_n, _ = states_ref.shape
    for c in range(spans):
        wide = states_ref[c].astype(jnp.float32)
        column = jnp.sum(wide * wide, axis=1, keepdims=True)
        squares_ref[pl.ds(c, 1), :] = jnp.transpose(jnp.broadcast_to(column, (slots_n, 128)))[:1, :]


def make_local(dp_shape):
    groups = dp_shape[0] * dp_shape[1] * dp_shape[2]

    def local(states, valid_counts, section_ids, norm_gain, head_weight):
        local_spans, slots_n, features = states.shape
        partial_squares = pl.pallas_call(
            squares_kernel,
            out_shape=pltpu.VMEM((local_spans, slots_n), jnp.float32),
            out_specs=pl.BlockSpec(memory_space=pltpu.VMEM),
        )(states)
        squares = fsdp_sum(partial_squares)
        local_spans, slots_n, features = states.shape
        sec_local = local_spans // 2
        total_sections = sec_local * groups
        smem = pl.BlockSpec(memory_space=pltpu.SMEM)
        vmem = pl.BlockSpec(memory_space=pltpu.VMEM)
        contrib = pl.pallas_call(
            functools.partial(pool_kernel, dp_shape),
            out_shape=pltpu.VMEM((total_sections, 1, features), jnp.float32),
            grid=(local_spans,),
            in_specs=[
                smem,
                smem,
                pl.BlockSpec((1, slots_n, features), lambda c: (c, 0, 0)),
                pl.BlockSpec((local_spans, slots_n), lambda c: (0, 0), memory_space=pltpu.VMEM),
            ],
            out_specs=pl.BlockSpec((total_sections, 1, features), lambda c: (0, 0, 0), memory_space=pltpu.VMEM),
        )(valid_counts, section_ids, states, pltpu.with_memory_space_constraint(squares, pltpu.VMEM))
        received = lax.all_to_all(contrib, ("c", "xh", "z"), 0, 0, tiled=True)
        section_sums = jnp.sum(received.reshape(groups, sec_local, features), axis=0)
        section_sums = section_sums * norm_gain.astype(jnp.float32)[None, :]
        parts = split3_rounded(section_sums)
        stacked = jnp.dot(parts.reshape(-1, features), head_weight, preferred_element_type=jnp.float32)
        terms = jnp.sum(stacked.reshape(3, sec_local, -1), axis=0)
        projected = fsdp_sum(terms)
        return nested(projected)

    return local


def solution(mesh):
    dp, fsdp = mesh.shape["dp"], mesh.shape["fsdp"]
    dp_shape = (dp // 4, 2, 2)
    fine = Mesh(mesh.devices.reshape(*dp_shape, 2, fsdp // 2), ("z", "xh", "c", "xl", "y"))
    spans = ("z", "xh", "c")
    features = ("xl", "y")
    in_specs = (P(spans, None, features), P(spans), P(), P(features), P(features, None))
    out_specs = P(spans, None)
    return jax.shard_map(make_local(dp_shape), mesh=fine, in_specs=in_specs, out_specs=out_specs, check_vma=False)
```
